256 devices in a mesh: space: 16 (over x_hi, z), chan: 8 (over y, core), dp: 2 (over x_lo).
Axes of the slice: x: 4 (x_hi: 2, x_lo: 2; x = x_hi * 2 + x_lo), y: 4, z: 8, core: 2. Of those that a mesh axis runs over, the one named last changes fastest.
Arguments:
- inputs: bfloat16 [2, 32, 8, 128, 512], P('dp', 'space', None, 'chan'), may hold values from -6 to 6
- cotangent: bfloat16 [2, 32, 8, 128, 512], P('dp', 'space', None, 'chan'), may hold values from -6 to 6
- weight: bfloat16 [27, 128, 128], P(None, 'chan'), may hold values from -0.109375 to 0.109375
Outputs:
- input_grad: bfloat16 [2, 32, 8, 128, 512], P('dp', 'space', None, 'chan')
- weight_grad: float32 [27, 128, 128], P(None, 'chan')
The draws below stay inside these ranges and needn't reach their ends.
All inputs are finite; a program needn't handle non-finite values.
Results may differ from the reference program's by a relative error of at most 0.001.
Values may be sent and summed in bfloat16 or wider, within the bound.
No kernel may reach another device: no remote copies, remote signals or barrier semaphores. Data moves between devices by JAX's collectives and lax.ppermute only.
A program may use at most 64 MiB of HBM per device.

```python
import math
import jax
import jax.numpy as jnp
from jax import lax

CIN = 128
COUT = 128
ZC = 8
YC = 512
BATCH = 2
NX = 32


def shard_levels(key, dims, shards, least, high):
    level, own = 1.0, jax.random.fold_in(key, 6)
    for position, shards_of in shards:
        heights = jnp.exp(jax.random.uniform(jax.random.fold_in(own, position), (shards_of,), jnp.float32, least / len(shards), high / len(shards)))
        level = level * jnp.repeat(heights, dims[position] // shards_of).reshape([-1 if axis == position else 1 for axis in range(len(dims))])
    return level


def bell_draw(rng, dims, deviation, reach, cuts=(), kind=jnp.bfloat16):
    entries = deviation * jax.random.normal(rng, dims, jnp.float32)
    if cuts:
        entries = entries * shard_levels(rng, dims, cuts, -0.22, 0.18)
    return jnp.clip(entries, -reach, reach).astype(kind)


def setup_inputs(seed: int = 0) -> dict:
    key_list = jax.random.split(jax.random.key(seed), 4)
    inputs = bell_draw(key_list[0], (BATCH, NX, ZC, CIN, YC), 1.0, 6.0, ((0, 2), (1, 16), (3, 8)))
    cotangent = bell_draw(key_list[1], (BATCH, NX, ZC, COUT, YC), 1.0, 6.0, ((0, 2), (1, 16), (3, 8)))
    weight = bell_draw(key_list[2], (27, CIN, COUT), (27 * CIN) ** -0.5, 0.109375, ((1, 8),))
    return dict(inputs=inputs, cotangent=cotangent, weight=weight)


def moved(block, step_x, step_z, step_y):
    zero = jnp.zeros((), block.dtype)
    config = ((0, 0, 0), (step_x, -step_x, 0), (step_z, -step_z, 0), (0, 0, 0), (step_y, -step_y, 0))
    return lax.pad(block, zero, config)

def reference(inputs, cotangent, weight):
    source = inputs.astype(jnp.float32)
    grads = cotangent.astype(jnp.float32)
    kernel = weight.astype(jnp.float32)
    batch, planes, depth, channels, width = inputs.shape
    scale = 1.0 / math.sqrt(batch * planes * depth * width)
    input_grad = jnp.zeros(inputs.shape, jnp.float32)
    pieces = []
    for step_x in (-1, 0, 1):
        for step_z in (-1, 0, 1):
            for step_y in (-1, 0, 1):
                index = 9 * (step_x + 1) + 3 * (step_z + 1) + step_y + 1
                product = jnp.einsum('bxzcy,ic->bxziy', grads, kernel[index], precision=lax.Precision.HIGHEST)
                input_grad = input_grad + moved(product, step_x, step_z, step_y)
                shifted = moved(source, -step_x, -step_z, -step_y)
                pieces.append(jnp.einsum('bxziy,bxzcy->ic', shifted, grads, precision=lax.Precision.HIGHEST))
    weight_grad = jnp.stack(pieces) * scale
    return (input_grad.astype(jnp.bfloat16), weight_grad)
```

```python
import math

import jax
import jax.numpy as jnp
from jax import lax
from jax.sharding import PartitionSpec as P


def from_behind(value, axis, steps):
    count = lax.axis_size(axis)
    initial, last = (max(0, -steps), min(count, count - steps))
    return lax.ppermute(value, axis, [(source, source + steps) for source in range(initial, last)])


def exchange_sum(value, axis, distance):
    count = lax.axis_size(axis)
    return value + lax.ppermute(value, axis, [(i, i ^ distance) for i in range(count)])


def butterfly_sum(value):
    value = exchange_sum(value, "dp", 1)
    for distance in (1, 8, 2, 4):
        value = exchange_sum(value, "space", distance)
    return value


def shift_cells(block, step_z, step_y):
    zero = jnp.zeros((), block.dtype)
    config = ((0, 0, 0), (0, 0, 0), (step_z, -step_z, 0), (0, 0, 0), (step_y, -step_y, 0))
    return lax.pad(block, zero, config)


def local(inputs, cotangent, weight):
    samples, planes, depth, channels, width = inputs.shape
    outputs = weight.shape[2]
    gathered = lax.all_gather(cotangent, "chan", axis=3, tiled=True)
    lower_plane = from_behind(gathered[:, -1:], "space", 1)
    upper_plane = from_behind(gathered[:, :1], "space", -1)
    stacked = jnp.concatenate(
        [shift_cells(inputs, -step_z, -step_y) for step_z in (-1, 0, 1) for step_y in (-1, 0, 1)],
        axis=3,
    )
    accum = jnp.zeros(inputs.shape, jnp.float32)
    groups = []
    for step_x in (-1, 0, 1):
        if step_x == 1:
            slab = jnp.concatenate([lower_plane, gathered[:, : planes - 1]], axis=1)
        elif step_x == -1:
            slab = jnp.concatenate([gathered[:, 1:], upper_plane], axis=1)
        else:
            slab = gathered
        first = 9 * (step_x + 1)
        groups.append(
            jnp.einsum("bxzky,bxzcy->kc", stacked, slab, preferred_element_type=jnp.float32)
        )
        for step_y in (-1, 0, 1):
            kernel = weight[first + step_y + 1 : first + 9 : 3].reshape(3 * channels, outputs)
            product = jnp.einsum(
                "bxzcy,kc->bxzky", slab, kernel, preferred_element_type=jnp.float32
            )
            for place, step_z in enumerate((-1, 0, 1)):
                part = product[:, :, :, place * channels : (place + 1) * channels]
                accum = accum + shift_cells(part, step_z, step_y)
    input_grad = accum.astype(jnp.bfloat16)
    local_grad = jnp.concatenate(groups, axis=0).reshape(27, channels, outputs)
    count = samples * lax.axis_size("dp") * planes * lax.axis_size("space") * depth * width
    scale = 1.0 / math.sqrt(count)
    weight_grad = butterfly_sum(local_grad) * scale
    return (input_grad, weight_grad)


def solution(mesh):
    placed = (
        P("dp", "space", None, "chan", None),
        P("dp", "space", None, "chan", None),
        P(None, "chan", None),
    )
    return jax.shard_map(
        local,
        mesh=mesh,
        in_specs=placed,
        out_specs=(P("dp", "space", None, "chan", None), P(None, "chan", None)),
        check_vma=False,
    )
```

```python
import math

import jax
import jax.numpy as jnp
from jax import lax
from jax.sharding import PartitionSpec as P


def from_behind(value, axis, steps):
    count = lax.axis_size(axis)
    initial, last = (max(0, -steps), min(count, count - steps))
    return lax.ppermute(value, axis, [(source, source + steps) for source in range(initial, last)])


def exchange_sum(value, axis, distance):
    count = lax.axis_size(axis)
    return value + lax.ppermute(value, axis, [(i, i ^ distance) for i in range(count)])


def butterfly_sum(value):
    value = exchange_sum(value, "dp", 1)
    for distance in (1, 8, 2, 4):
        value = exchange_sum(value, "space", distance)
    return value


def shift_cells(block, step_z, step_y):
    zero = jnp.zeros((), block.dtype)
    config = ((0, 0, 0), (0, 0, 0), (step_z, -step_z, 0), (0, 0, 0), (step_y, -step_y, 0))
    return lax.pad(block, zero, config)


def local(inputs, cotangent, weight):
    samples, planes, depth, channels, width = inputs.shape
    outputs = weight.shape[2]
    inputs_ext = jnp.concatenate(
        [from_behind(inputs[:, -1:], "space", 1), inputs, from_behind(inputs[:, :1], "space", -1)],
        axis=1,
    )
    cot_halo = jnp.concatenate(
        [from_behind(cotangent[:, -1:], "space", 1), from_behind(cotangent[:, :1], "space", -1)],
        axis=1,
    )
    gathered = lax.all_gather(cotangent, "chan", axis=3, tiled=True)
    stacked = jnp.concatenate(
        [shift_cells(inputs_ext, -step_z, -step_y) for step_z in (-1, 0, 1) for step_y in (-1, 0, 1)],
        axis=3,
    )
    groups = []
    for step_x in (-1, 0, 1):
        source = stacked[:, 1 + step_x : 1 + step_x + planes]
        groups.append(
            jnp.einsum("bxzky,bxzcy->kc", source, gathered, preferred_element_type=jnp.float32)
        )
    local_grad = jnp.concatenate(groups, axis=0).reshape(27, channels, outputs)
    count = samples * lax.axis_size("dp") * planes * lax.axis_size("space") * depth * width
    scale = 1.0 / math.sqrt(count)
    weight_grad = butterfly_sum(local_grad) * scale

    halo = lax.all_gather(cot_halo, "chan", axis=3, tiled=True)
    lower_plane, upper_plane = halo[:, :1], halo[:, 1:]
    accum = jnp.zeros(inputs.shape, jnp.float32)
    for step_x in (-1, 0, 1):
        if step_x == 1:
            slab = jnp.concatenate([lower_plane, gathered[:, : planes - 1]], axis=1)
        elif step_x == -1:
            slab = jnp.concatenate([gathered[:, 1:], upper_plane], axis=1)
        else:
            slab = gathered
        first = 9 * (step_x + 1)
        for step_y in (-1, 0, 1):
            kernel = weight[first + step_y + 1 : first + 9 : 3].reshape(3 * channels, outputs)
            product = jnp.einsum(
                "bxzcy,kc->bxzky", slab, kernel, preferred_element_type=jnp.float32
            )
            for place, step_z in enumerate((-1, 0, 1)):
                part = product[:, :, :, place * channels : (place + 1) * channels]
                accum = accum + shift_cells(part, step_z, step_y)
    input_grad = accum.astype(jnp.bfloat16)
    return (input_grad, weight_grad)


def solution(mesh):
    placed = (
        P("dp", "space", None, "chan", None),
        P("dp", "space", None, "chan", None),
        P(None, "chan", None),
    )
    return jax.shard_map(
        local,
        mesh=mesh,
        in_specs=placed,
        out_specs=(P("dp", "space", None, "chan", None), P(None, "chan", None)),
        check_vma=False,
    )
```

```python
import math

import jax
import jax.numpy as jnp
from jax import lax
from jax.sharding import PartitionSpec as P


def from_behind(value, axis, steps):
    count = lax.axis_size(axis)
    initial, last = (max(0, -steps), min(count, count - steps))
    return lax.ppermute(value, axis, [(source, source + steps) for source in range(initial, last)])


def exchange_sum(value, axis, distance):
    count = lax.axis_size(axis)
    return value + lax.ppermute(value, axis, [(i, i ^ distance) for i in range(count)])


def butterfly_sum(value):
    value = exchange_sum(value, "dp", 1)
    for distance in (1, 8, 2, 4):
        value = exchange_sum(value, "space", distance)
    return value


def shift_cells(block, step_z, step_y):
    zero = jnp.zeros((), block.dtype)
    config = ((0, 0, 0), (0, 0, 0), (step_z, -step_z, 0), (0, 0, 0), (step_y, -step_y, 0))
    return lax.pad(block, zero, config)


def local(inputs, cotangent, weight):
    samples, planes, depth, channels, width = inputs.shape
    outputs = weight.shape[2]
    inputs_ext = jnp.concatenate(
        [from_behind(inputs[:, -1:], "space", 1), inputs, from_behind(inputs[:, :1], "space", -1)],
        axis=1,
    )
    gathered = lax.all_gather(cotangent, "chan", axis=3, tiled=True)
    stacked = jnp.concatenate(
        [shift_cells(inputs_ext, -step_z, -step_y) for step_z in (-1, 0, 1) for step_y in (-1, 0, 1)],
        axis=3,
    )
    groups = []
    for step_x in (-1, 0, 1):
        source = stacked[:, 1 + step_x : 1 + step_x + planes]
        groups.append(
            jnp.einsum("bxzky,bxzcy->kc", source, gathered, preferred_element_type=jnp.float32)
        )
    local_grad = jnp.concatenate(groups, axis=0).reshape(27, channels, outputs)
    count = samples * lax.axis_size("dp") * planes * lax.axis_size("space") * depth * width
    scale = 1.0 / math.sqrt(count)
    weight_grad = butterfly_sum(local_grad) * scale

    contrib = {}
    for step_x in (-1, 0, 1):
        first = 9 * (step_x + 1)
        total = None
        for step_y in (-1, 0, 1):
            kernel = weight[first + step_y + 1 : first + 9 : 3].reshape(3 * channels, outputs)
            product = jnp.einsum(
                "bxzcy,kc->bxzky", gathered, kernel, preferred_element_type=jnp.float32
            )
            for place, step_z in enumerate((-1, 0, 1)):
                part = shift_cells(product[:, :, :, place * channels : (place + 1) * channels], step_z, step_y)
                total = part if total is None else total + part
        contrib[step_x] = total
    from_prev = from_behind(contrib[1][:, -1:], "space", 1)
    from_next = from_behind(contrib[-1][:, :1], "space", -1)
    accum = (
        contrib[0]
        + jnp.concatenate([from_prev, contrib[1][:, : planes - 1]], axis=1)
        + jnp.concatenate([contrib[-1][:, 1:], from_next], axis=1)
    )
    input_grad = accum.astype(jnp.bfloat16)
    return (input_grad, weight_grad)


def solution(mesh):
    placed = (
        P("dp", "space", None, "chan", None),
        P("dp", "space", None, "chan", None),
        P(None, "chan", None),
    )
    return jax.shard_map(
        local,
        mesh=mesh,
        in_specs=placed,
        out_specs=(P("dp", "space", None, "chan", None), P(None, "chan", None)),
        check_vma=False,
    )
```

```python
import math

import jax
import jax.numpy as jnp
from jax import lax
from jax.sharding import PartitionSpec as P


def from_behind(value, axis, steps):
    count = lax.axis_size(axis)
    initial, last = (max(0, -steps), min(count, count - steps))
    return lax.ppermute(value, axis, [(source, source + steps) for source in range(initial, last)])


def exchange_sum(value, axis, distance):
    count = lax.axis_size(axis)
    return value + lax.ppermute(value, axis, [(i, i ^ distance) for i in range(count)])


def butterfly_sum(value):
    value = exchange_sum(value, "dp", 1)
    for distance in (1, 8, 2, 4):
        value = exchange_sum(value, "space", distance)
    return value


def gather_channels(block, axis):
    count = lax.axis_size(axis)
    own = [block] + [
        lax.ppermute(block, axis, [(i, (i + 2 * step) % count) for i in range(count)])
        for step in range(1, count // 2)
    ]
    own = jnp.stack(own)
    partner = lax.ppermute(own, axis, [(i, i ^ 1) for i in range(count)])
    index = lax.axis_index(axis)
    sources = jnp.stack(
        [(index - 2 * step) % count for step in range(count // 2)]
        + [((index ^ 1) - 2 * step) % count for step in range(count // 2)]
    )
    blocks = jnp.concatenate([own, partner], axis=0)
    return blocks, sources


def shift_cells(block, step_z, step_y):
    zero = jnp.zeros((), block.dtype)
    config = ((0, 0, 0), (0, 0, 0), (step_z, -step_z, 0), (0, 0, 0), (step_y, -step_y, 0))
    return lax.pad(block, zero, config)


def local(inputs, cotangent, weight):
    samples, planes, depth, channels, width = inputs.shape
    outputs = weight.shape[2]
    inputs_ext = jnp.concatenate(
        [from_behind(inputs[:, -1:], "space", 1), inputs, from_behind(inputs[:, :1], "space", -1)],
        axis=1,
    )
    blocks, sources = gather_channels(cotangent, "chan")
    count = blocks.shape[0]
    gathered = jnp.concatenate(list(blocks), axis=3)
    weight = jnp.take(weight.reshape(27, channels, count, -1), sources, axis=2).reshape(weight.shape)
    stacked = jnp.concatenate(
        [shift_cells(inputs_ext, -step_z, -step_y) for step_z in (-1, 0, 1) for step_y in (-1, 0, 1)],
        axis=3,
    )
    groups = []
    for step_x in (-1, 0, 1):
        source = stacked[:, 1 + step_x : 1 + step_x + planes]
        groups.append(
            jnp.einsum("bxzky,bxzcy->kc", source, gathered, preferred_element_type=jnp.float32)
        )
    local_grad = jnp.concatenate(groups, axis=0).reshape(27, channels, count, -1)
    local_grad = jnp.take(local_grad, jnp.argsort(sources), axis=2).reshape(27, channels, outputs)
    count = samples * lax.axis_size("dp") * planes * lax.axis_size("space") * depth * width
    scale = 1.0 / math.sqrt(count)
    weight_grad = butterfly_sum(local_grad) * scale

    contrib = {}
    for step_x in (-1, 0, 1):
        first = 9 * (step_x + 1)
        total = None
        for step_y in (-1, 0, 1):
            kernel = weight[first + step_y + 1 : first + 9 : 3].reshape(3 * channels, outputs)
            product = jnp.einsum(
                "bxzcy,kc->bxzky", gathered, kernel, preferred_element_type=jnp.float32
            )
            for place, step_z in enumerate((-1, 0, 1)):
                part = shift_cells(product[:, :, :, place * channels : (place + 1) * channels], step_z, step_y)
                total = part if total is None else total + part
        contrib[step_x] = total
    from_prev = from_behind(contrib[1][:, -1:], "space", 1)
    from_next = from_behind(contrib[-1][:, :1], "space", -1)
    accum = (
        contrib[0]
        + jnp.concatenate([from_prev, contrib[1][:, : planes - 1]], axis=1)
        + jnp.concatenate([contrib[-1][:, 1:], from_next], axis=1)
    )
    input_grad = accum.astype(jnp.bfloat16)
    return (input_grad, weight_grad)


def solution(mesh):
    placed = (
        P("dp", "space", None, "chan", None),
        P("dp", "space", None, "chan", None),
        P(None, "chan", None),
    )
    return jax.shard_map(
        local,
        mesh=mesh,
        in_specs=placed,
        out_specs=(P("dp", "space", None, "chan", None), P(None, "chan", None)),
        check_vma=False,
    )
```

```python
import math

import jax
import jax.numpy as jnp
from jax import lax
from jax.sharding import PartitionSpec as P


def from_behind(value, axis, steps):
    count = lax.axis_size(axis)
    initial, last = (max(0, -steps), min(count, count - steps))
    return lax.ppermute(value, axis, [(source, source + steps) for source in range(initial, last)])


def exchange_sum(value, axis, distance):
    count = lax.axis_size(axis)
    return value + lax.ppermute(value, axis, [(i, i ^ distance) for i in range(count)])


def butterfly_sum(value, order):
    for axis, distance in order:
        value = exchange_sum(value, axis, distance)
    return value


def split_sum(value):
    half = value.shape[0] // 2
    first = butterfly_sum(value[:half], (("dp", 1), ("space", 1), ("space", 8), ("space", 2), ("space", 4)))
    second = butterfly_sum(value[half:], (("space", 1), ("space", 2), ("space", 4), ("dp", 1), ("space", 8)))
    return jnp.concatenate([first, second], axis=0)


def gather_channels(block, axis):
    count = lax.axis_size(axis)
    own = [block] + [
        lax.ppermute(block, axis, [(i, (i + 2 * step) % count) for i in range(count)])
        for step in range(1, count // 2)
    ]
    own = jnp.stack(own)
    partner = lax.ppermute(own, axis, [(i, i ^ 1) for i in range(count)])
    index = lax.axis_index(axis)
    sources = jnp.stack(
        [(index - 2 * step) % count for step in range(count // 2)]
        + [((index ^ 1) - 2 * step) % count for step in range(count // 2)]
    )
    blocks = jnp.concatenate([own, partner], axis=0)
    return blocks, sources


def shift_cells(block, step_z, step_y):
    zero = jnp.zeros((), block.dtype)
    config = ((0, 0, 0), (0, 0, 0), (step_z, -step_z, 0), (0, 0, 0), (step_y, -step_y, 0))
    return lax.pad(block, zero, config)


def local(inputs, cotangent, weight):
    samples, planes, depth, channels, width = inputs.shape
    outputs = weight.shape[2]
    inputs_ext = jnp.concatenate(
        [from_behind(inputs[:, -1:], "space", 1), inputs, from_behind(inputs[:, :1], "space", -1)],
        axis=1,
    )
    blocks, sources = gather_channels(cotangent, "chan")
    count = blocks.shape[0]
    gathered = jnp.zeros(blocks.shape[1:4] + (count * channels,) + blocks.shape[5:], blocks.dtype)
    for place in range(count):
        gathered = lax.dynamic_update_slice_in_dim(gathered, blocks[place], sources[place] * channels, axis=3)
    stacked = jnp.concatenate(
        [shift_cells(inputs_ext, -step_z, -step_y) for step_z in (-1, 0, 1) for step_y in (-1, 0, 1)],
        axis=3,
    )
    groups = []
    for step_x in (-1, 0, 1):
        source = stacked[:, 1 + step_x : 1 + step_x + planes]
        groups.append(
            jnp.einsum("bxzky,bxzcy->kc", source, gathered, preferred_element_type=jnp.float32)
        )
    local_grad = jnp.concatenate(groups, axis=0).reshape(27, channels, outputs)
    count = samples * lax.axis_size("dp") * planes * lax.axis_size("space") * depth * width
    scale = 1.0 / math.sqrt(count)
    weight_grad = split_sum(local_grad.reshape(-1, outputs)).reshape(local_grad.shape) * scale

    contrib = {}
    for step_x in (-1, 0, 1):
        first = 9 * (step_x + 1)
        total = None
        for step_y in (-1, 0, 1):
            kernel = weight[first + step_y + 1 : first + 9 : 3].reshape(3 * channels, outputs)
            product = jnp.einsum(
                "bxzcy,kc->bxzky", gathered, kernel, preferred_element_type=jnp.float32
            )
            for place, step_z in enumerate((-1, 0, 1)):
                part = shift_cells(product[:, :, :, place * channels : (place + 1) * channels], step_z, step_y)
                total = part if total is None else total + part
        contrib[step_x] = total
    from_prev = from_behind(contrib[1][:, -1:], "space", 1)
    from_next = from_behind(contrib[-1][:, :1], "space", -1)
    accum = (
        contrib[0]
        + jnp.concatenate([from_prev, contrib[1][:, : planes - 1]], axis=1)
        + jnp.concatenate([contrib[-1][:, 1:], from_next], axis=1)
    )
    input_grad = accum.astype(jnp.bfloat16)
    return (input_grad, weight_grad)


def solution(mesh):
    placed = (
        P("dp", "space", None, "chan", None),
        P("dp", "space", None, "chan", None),
        P(None, "chan", None),
    )
    return jax.shard_map(
        local,
        mesh=mesh,
        in_specs=placed,
        out_specs=(P("dp", "space", None, "chan", None), P(None, "chan", None)),
        check_vma=False,
    )
```

```python
import math

import jax
import jax.numpy as jnp
from jax import lax
from jax.sharding import PartitionSpec as P


def from_behind(value, axis, steps):
    count = lax.axis_size(axis)
    initial, last = (max(0, -steps), min(count, count - steps))
    return lax.ppermute(value, axis, [(source, source + steps) for source in range(initial, last)])


def exchange_sum(value, axis, distance):
    count = lax.axis_size(axis)
    return value + lax.ppermute(value, axis, [(i, i ^ distance) for i in range(count)])


def group_sum(value, axes, masks):
    count = lax.axis_size(axes)
    index = lax.axis_index(axes)
    members = 1 << len(masks)
    place = sum(((index & mask) != 0).astype(jnp.int32) << bit for bit, mask in enumerate(masks))
    received = [value]
    for member in range(1, members):
        flip = 0
        for bit, mask in enumerate(masks):
            if member >> bit & 1:
                flip ^= mask
        received.append(lax.ppermute(value, axes, [(i, i ^ flip) for i in range(count)]))
    ordered = []
    for member in range(members):
        choice = received[0]
        for other in range(1, members):
            choice = jnp.where((place ^ member) == other, received[other], choice)
        ordered.append(choice)
    while len(ordered) > 1:
        ordered = [ordered[k] + ordered[k + 1] for k in range(0, len(ordered), 2)]
    return ordered[0]


def group_reduce(value):
    axes = ("space", "dp")
    value = group_sum(value, axes, (1, 2))
    value = group_sum(value, axes, (4, 16))
    return group_sum(value, axes, (8,))


def gather_channels(block, axis):
    count = lax.axis_size(axis)
    own = [block] + [
        lax.ppermute(block, axis, [(i, (i + 2 * step) % count) for i in range(count)])
        for step in range(1, count // 2)
    ]
    own = jnp.stack(own)
    partner = lax.ppermute(own, axis, [(i, i ^ 1) for i in range(count)])
    index = lax.axis_index(axis)
    sources = jnp.stack(
        [(index - 2 * step) % count for step in range(count // 2)]
        + [((index ^ 1) - 2 * step) % count for step in range(count // 2)]
    )
    blocks = jnp.concatenate([own, partner], axis=0)
    return blocks, sources


def shift_cells(block, step_z, step_y):
    zero = jnp.zeros((), block.dtype)
    config = ((0, 0, 0), (0, 0, 0), (step_z, -step_z, 0), (0, 0, 0), (step_y, -step_y, 0))
    return lax.pad(block, zero, config)


def local(inputs, cotangent, weight):
    samples, planes, depth, channels, width = inputs.shape
    outputs = weight.shape[2]
    inputs_ext = jnp.concatenate(
        [from_behind(inputs[:, -1:], "space", 1), inputs, from_behind(inputs[:, :1], "space", -1)],
        axis=1,
    )
    blocks, sources = gather_channels(cotangent, "chan")
    count = blocks.shape[0]
    gathered = jnp.zeros(blocks.shape[1:4] + (count * channels,) + blocks.shape[5:], blocks.dtype)
    for place in range(count):
        gathered = lax.dynamic_update_slice_in_dim(gathered, blocks[place], sources[place] * channels, axis=3)
    stacked = jnp.concatenate(
        [shift_cells(inputs_ext, -step_z, -step_y) for step_z in (-1, 0, 1) for step_y in (-1, 0, 1)],
        axis=3,
    )
    groups = []
    for step_x in (-1, 0, 1):
        source = stacked[:, 1 + step_x : 1 + step_x + planes]
        groups.append(
            jnp.einsum("bxzky,bxzcy->kc", source, gathered, preferred_element_type=jnp.float32)
        )
    local_grad = jnp.concatenate(groups, axis=0).reshape(27, channels, outputs)
    count = samples * lax.axis_size("dp") * planes * lax.axis_size("space") * depth * width
    scale = 1.0 / math.sqrt(count)
    weight_grad = group_reduce(local_grad.reshape(-1, outputs)).reshape(local_grad.shape) * scale

    contrib = {}
    for step_x in (-1, 0, 1):
        first = 9 * (step_x + 1)
        total = None
        for step_y in (-1, 0, 1):
            kernel = weight[first + step_y + 1 : first + 9 : 3].reshape(3 * channels, outputs)
            product = jnp.einsum(
                "bxzcy,kc->bxzky", gathered, kernel, preferred_element_type=jnp.float32
            )
            for place, step_z in enumerate((-1, 0, 1)):
                part = shift_cells(product[:, :, :, place * channels : (place + 1) * channels], step_z, step_y)
                total = part if total is None else total + part
        contrib[step_x] = total
    from_prev = from_behind(contrib[1][:, -1:], "space", 1)
    from_next = from_behind(contrib[-1][:, :1], "space", -1)
    accum = (
        contrib[0]
        + jnp.concatenate([from_prev, contrib[1][:, : planes - 1]], axis=1)
        + jnp.concatenate([contrib[-1][:, 1:], from_next], axis=1)
    )
    input_grad = accum.astype(jnp.bfloat16)
    return (input_grad, weight_grad)


def solution(mesh):
    placed = (
        P("dp", "space", None, "chan", None),
        P("dp", "space", None, "chan", None),
        P(None, "chan", None),
    )
    return jax.shard_map(
        local,
        mesh=mesh,
        in_specs=placed,
        out_specs=(P("dp", "space", None, "chan", None), P(None, "chan", None)),
        check_vma=False,
    )
```

```python
import math

import jax
import jax.numpy as jnp
from jax import lax
from jax.sharding import PartitionSpec as P


def from_behind(value, axis, steps):
    count = lax.axis_size(axis)
    initial, last = (max(0, -steps), min(count, count - steps))
    return lax.ppermute(value, axis, [(source, source + steps) for source in range(initial, last)])


def exchange_sum(value, axis, distance):
    count = lax.axis_size(axis)
    return value + lax.ppermute(value, axis, [(i, i ^ distance) for i in range(count)])


def group_sum(value, axes, masks):
    count = lax.axis_size(axes)
    index = lax.axis_index(axes)
    members = 1 << len(masks)
    place = sum(((index & mask) != 0).astype(jnp.int32) << bit for bit, mask in enumerate(masks))
    received = [value]
    for member in range(1, members):
        flip = 0
        for bit, mask in enumerate(masks):
            if member >> bit & 1:
                flip ^= mask
        received.append(lax.ppermute(value, axes, [(i, i ^ flip) for i in range(count)]))
    ordered = []
    for member in range(members):
        choice = received[0]
        for other in range(1, members):
            choice = jnp.where((place ^ member) == other, received[other], choice)
        ordered.append(choice)
    while len(ordered) > 1:
        ordered = [ordered[k] + ordered[k + 1] for k in range(0, len(ordered), 2)]
    return ordered[0]


def flip_of(member, masks):
    flip = 0
    for bit, mask in enumerate(masks):
        if member >> bit & 1:
            flip ^= mask
    return flip


def pick(choices, selector):
    choice = choices[0]
    for other in range(1, len(choices)):
        choice = jnp.where(selector == other, choices[other], choice)
    return choice


def group_reduce(value):
    axes = ("space", "dp")
    masks = (1, 2)
    count = lax.axis_size(axes)
    index = lax.axis_index(axes)
    members = 1 << len(masks)
    place = sum(((index & mask) != 0).astype(jnp.int32) << bit for bit, mask in enumerate(masks))
    chunks = value.reshape((members, -1) + value.shape[1:])
    received = [chunks[0]]
    for member in range(1, members):
        pairs = [(i, i ^ flip_of(member, masks)) for i in range(count)]
        send = lax.dynamic_index_in_dim(chunks, place ^ member, axis=0, keepdims=False)
        received.append(lax.ppermute(send, axes, pairs))
    own = lax.dynamic_index_in_dim(chunks, place, axis=0, keepdims=False)
    received[0] = own
    ordered = [pick(received, place ^ member) for member in range(members)]
    while len(ordered) > 1:
        ordered = [ordered[k] + ordered[k + 1] for k in range(0, len(ordered), 2)]
    part = group_sum(ordered[0], axes, (4, 16))
    part = group_sum(part, axes, (8,))
    pieces = [part] + [
        lax.ppermute(part, axes, [(i, i ^ flip_of(member, masks)) for i in range(count)])
        for member in range(1, members)
    ]
    whole = [pick(pieces, place ^ member) for member in range(members)]
    return jnp.concatenate(whole, axis=0)


def gather_channels(block, axis):
    count = lax.axis_size(axis)
    own = [block] + [
        lax.ppermute(block, axis, [(i, (i + 2 * step) % count) for i in range(count)])
        for step in range(1, count // 2)
    ]
    own = jnp.stack(own)
    partner = lax.ppermute(own, axis, [(i, i ^ 1) for i in range(count)])
    index = lax.axis_index(axis)
    sources = jnp.stack(
        [(index - 2 * step) % count for step in range(count // 2)]
        + [((index ^ 1) - 2 * step) % count for step in range(count // 2)]
    )
    blocks = jnp.concatenate([own, partner], axis=0)
    return blocks, sources


def shift_cells(block, step_z, step_y):
    zero = jnp.zeros((), block.dtype)
    config = ((0, 0, 0), (0, 0, 0), (step_z, -step_z, 0), (0, 0, 0), (step_y, -step_y, 0))
    return lax.pad(block, zero, config)


def local(inputs, cotangent, weight):
    samples, planes, depth, channels, width = inputs.shape
    outputs = weight.shape[2]
    inputs_ext = jnp.concatenate(
        [from_behind(inputs[:, -1:], "space", 1), inputs, from_behind(inputs[:, :1], "space", -1)],
        axis=1,
    )
    blocks, sources = gather_channels(cotangent, "chan")
    count = blocks.shape[0]
    gathered = jnp.zeros(blocks.shape[1:4] + (count * channels,) + blocks.shape[5:], blocks.dtype)
    for place in range(count):
        gathered = lax.dynamic_update_slice_in_dim(gathered, blocks[place], sources[place] * channels, axis=3)
    stacked = jnp.concatenate(
        [shift_cells(inputs_ext, -step_z, -step_y) for step_z in (-1, 0, 1) for step_y in (-1, 0, 1)],
        axis=3,
    )
    groups = []
    for step_x in (-1, 0, 1):
        source = stacked[:, 1 + step_x : 1 + step_x + planes]
        groups.append(
            jnp.einsum("bxzky,bxzcy->kc", source, gathered, preferred_element_type=jnp.float32)
        )
    local_grad = jnp.concatenate(groups, axis=0).reshape(27, channels, outputs)
    count = samples * lax.axis_size("dp") * planes * lax.axis_size("space") * depth * width
    scale = 1.0 / math.sqrt(count)
    weight_grad = group_reduce(local_grad.reshape(-1, outputs)).reshape(local_grad.shape) * scale

    contrib = {}
    for step_x in (-1, 0, 1):
        first = 9 * (step_x + 1)
        total = None
        for step_y in (-1, 0, 1):
            kernel = weight[first + step_y + 1 : first + 9 : 3].reshape(3 * channels, outputs)
            product = jnp.einsum(
                "bxzcy,kc->bxzky", gathered, kernel, preferred_element_type=jnp.float32
            )
            for place, step_z in enumerate((-1, 0, 1)):
                part = shift_cells(product[:, :, :, place * channels : (place + 1) * channels], step_z, step_y)
                total = part if total is None else total + part
        contrib[step_x] = total
    from_prev = from_behind(contrib[1][:, -1:], "space", 1)
    from_next = from_behind(contrib[-1][:, :1], "space", -1)
    accum = (
        contrib[0]
        + jnp.concatenate([from_prev, contrib[1][:, : planes - 1]], axis=1)
        + jnp.concatenate([contrib[-1][:, 1:], from_next], axis=1)
    )
    input_grad = accum.astype(jnp.bfloat16)
    return (input_grad, weight_grad)


def solution(mesh):
    placed = (
        P("dp", "space", None, "chan", None),
        P("dp", "space", None, "chan", None),
        P(None, "chan", None),
    )
    return jax.shard_map(
        local,
        mesh=mesh,
        in_specs=placed,
        out_specs=(P("dp", "space", None, "chan", None), P(None, "chan", None)),
        check_vma=False,
    )
```

```python
import math

import jax
import jax.numpy as jnp
from jax import lax
from jax.sharding import PartitionSpec as P


def from_behind(value, axis, steps):
    count = lax.axis_size(axis)
    initial, last = (max(0, -steps), min(count, count - steps))
    return lax.ppermute(value, axis, [(source, source + steps) for source in range(initial, last)])


def exchange_sum(value, axis, distance):
    count = lax.axis_size(axis)
    return value + lax.ppermute(value, axis, [(i, i ^ distance) for i in range(count)])


def group_sum(value, axes, masks):
    count = lax.axis_size(axes)
    index = lax.axis_index(axes)
    members = 1 << len(masks)
    place = sum(((index & mask) != 0).astype(jnp.int32) << bit for bit, mask in enumerate(masks))
    received = [value]
    for member in range(1, members):
        flip = 0
        for bit, mask in enumerate(masks):
            if member >> bit & 1:
                flip ^= mask
        received.append(lax.ppermute(value, axes, [(i, i ^ flip) for i in range(count)]))
    ordered = []
    for member in range(members):
        choice = received[0]
        for other in range(1, members):
            choice = jnp.where((place ^ member) == other, received[other], choice)
        ordered.append(choice)
    while len(ordered) > 1:
        ordered = [ordered[k] + ordered[k + 1] for k in range(0, len(ordered), 2)]
    return ordered[0]


def flip_of(member, masks):
    flip = 0
    for bit, mask in enumerate(masks):
        if member >> bit & 1:
            flip ^= mask
    return flip


def pick(choices, selector):
    choice = choices[0]
    for other in range(1, len(choices)):
        choice = jnp.where(selector == other, choices[other], choice)
    return choice


def group_reduce(value):
    axes = ("space", "dp")
    masks = (1, 2)
    count = lax.axis_size(axes)
    index = lax.axis_index(axes)
    members = 1 << len(masks)
    place = sum(((index & mask) != 0).astype(jnp.int32) << bit for bit, mask in enumerate(masks))
    chunks = value.reshape((members, -1) + value.shape[1:])
    received = [chunks[0]]
    for member in range(1, members):
        pairs = [(i, i ^ flip_of(member, masks)) for i in range(count)]
        send = lax.dynamic_index_in_dim(chunks, place ^ member, axis=0, keepdims=False)
        received.append(lax.ppermute(send, axes, pairs))
    own = lax.dynamic_index_in_dim(chunks, place, axis=0, keepdims=False)
    received[0] = own
    ordered = [pick(received, place ^ member) for member in range(members)]
    while len(ordered) > 1:
        ordered = [ordered[k] + ordered[k + 1] for k in range(0, len(ordered), 2)]
    part = group_sum(ordered[0], axes, (4, 16))
    part = group_sum(part, axes, (8,))
    pieces = [part] + [
        lax.ppermute(part, axes, [(i, i ^ flip_of(member, masks)) for i in range(count)])
        for member in range(1, members)
    ]
    whole = [pick(pieces, place ^ member) for member in range(members)]
    return jnp.concatenate(whole, axis=0)


def gather_channels(block, axis):
    count = lax.axis_size(axis)
    own = [block] + [
        lax.ppermute(block, axis, [(i, (i + 2 * step) % count) for i in range(count)])
        for step in range(1, count // 2)
    ]
    own = jnp.stack(own)
    partner = lax.ppermute(own, axis, [(i, i ^ 1) for i in range(count)])
    index = lax.axis_index(axis)
    sources = jnp.stack(
        [(index - 2 * step) % count for step in range(count // 2)]
        + [((index ^ 1) - 2 * step) % count for step in range(count // 2)]
    )
    blocks = jnp.concatenate([own, partner], axis=0)
    return blocks, sources


def shift_cells(block, step_z, step_y):
    zero = jnp.zeros((), block.dtype)
    config = ((0, 0, 0), (0, 0, 0), (step_z, -step_z, 0), (0, 0, 0), (step_y, -step_y, 0))
    return lax.pad(block, zero, config)


def local(inputs, cotangent, weight):
    samples, planes, depth, channels, width = inputs.shape
    outputs = weight.shape[2]
    inputs_ext = jnp.concatenate(
        [from_behind(inputs[:, -1:], "space", 1), inputs, from_behind(inputs[:, :1], "space", -1)],
        axis=1,
    )
    blocks, sources = gather_channels(cotangent, "chan")
    count = blocks.shape[0]
    gathered = jnp.zeros(blocks.shape[1:4] + (count * channels,) + blocks.shape[5:], blocks.dtype)
    for place in range(count):
        gathered = lax.dynamic_update_slice_in_dim(gathered, blocks[place], sources[place] * channels, axis=3)
    contrib = {}
    for step_x in (-1, 0, 1):
        first = 9 * (step_x + 1)
        total = None
        for step_y in (-1, 0, 1):
            kernel = weight[first + step_y + 1 : first + 9 : 3].reshape(3 * channels, outputs)
            product = jnp.einsum(
                "bxzcy,kc->bxzky", gathered, kernel, preferred_element_type=jnp.float32
            )
            for place, step_z in enumerate((-1, 0, 1)):
                part = shift_cells(product[:, :, :, place * channels : (place + 1) * channels], step_z, step_y)
                total = part if total is None else total + part
        contrib[step_x] = total
    contrib, gathered = lax.optimization_barrier((contrib, gathered))
    stacked = jnp.concatenate(
        [shift_cells(inputs_ext, -step_z, -step_y) for step_z in (-1, 0, 1) for step_y in (-1, 0, 1)],
        axis=3,
    )
    groups = []
    for step_x in (-1, 0, 1):
        source = stacked[:, 1 + step_x : 1 + step_x + planes]
        groups.append(
            jnp.einsum("bxzky,bxzcy->kc", source, gathered, preferred_element_type=jnp.float32)
        )
    local_grad = jnp.concatenate(groups, axis=0).reshape(27, channels, outputs)
    count = samples * lax.axis_size("dp") * planes * lax.axis_size("space") * depth * width
    scale = 1.0 / math.sqrt(count)
    weight_grad = group_reduce(local_grad.reshape(-1, outputs)).reshape(local_grad.shape) * scale

    from_prev = from_behind(contrib[1][:, -1:], "space", 1)
    from_next = from_behind(contrib[-1][:, :1], "space", -1)
    accum = (
        contrib[0]
        + jnp.concatenate([from_prev, contrib[1][:, : planes - 1]], axis=1)
        + jnp.concatenate([contrib[-1][:, 1:], from_next], axis=1)
    )
    input_grad = accum.astype(jnp.bfloat16)
    return (input_grad, weight_grad)


def solution(mesh):
    placed = (
        P("dp", "space", None, "chan", None),
        P("dp", "space", None, "chan", None),
        P(None, "chan", None),
    )
    return jax.shard_map(
        local,
        mesh=mesh,
        in_specs=placed,
        out_specs=(P("dp", "space", None, "chan", None), P(None, "chan", None)),
        check_vma=False,
    )
```

```python
import math

import jax
import jax.numpy as jnp
from jax import lax
from jax.sharding import PartitionSpec as P


def from_behind(value, axis, steps):
    count = lax.axis_size(axis)
    initial, last = (max(0, -steps), min(count, count - steps))
    return lax.ppermute(value, axis, [(source, source + steps) for source in range(initial, last)])


def exchange_sum(value, axis, distance):
    count = lax.axis_size(axis)
    return value + lax.ppermute(value, axis, [(i, i ^ distance) for i in range(count)])


def group_sum(value, axes, masks):
    count = lax.axis_size(axes)
    index = lax.axis_index(axes)
    members = 1 << len(masks)
    place = sum(((index & mask) != 0).astype(jnp.int32) << bit for bit, mask in enumerate(masks))
    received = [value]
    for member in range(1, members):
        flip = 0
        for bit, mask in enumerate(masks):
            if member >> bit & 1:
                flip ^= mask
        received.append(lax.ppermute(value, axes, [(i, i ^ flip) for i in range(count)]))
    ordered = []
    for member in range(members):
        choice = received[0]
        for other in range(1, members):
            choice = jnp.where((place ^ member) == other, received[other], choice)
        ordered.append(choice)
    while len(ordered) > 1:
        ordered = [ordered[k] + ordered[k + 1] for k in range(0, len(ordered), 2)]
    return ordered[0]


def flip_of(member, masks):
    flip = 0
    for bit, mask in enumerate(masks):
        if member >> bit & 1:
            flip ^= mask
    return flip


def pick(choices, selector):
    choice = choices[0]
    for other in range(1, len(choices)):
        choice = jnp.where(selector == other, choices[other], choice)
    return choice


def group_reduce(value):
    axes = ("space", "dp")
    masks = (1, 2)
    count = lax.axis_size(axes)
    index = lax.axis_index(axes)
    members = 1 << len(masks)
    place = sum(((index & mask) != 0).astype(jnp.int32) << bit for bit, mask in enumerate(masks))
    chunks = value.reshape((members, -1) + value.shape[1:])
    received = [chunks[0]]
    for member in range(1, members):
        pairs = [(i, i ^ flip_of(member, masks)) for i in range(count)]
        send = lax.dynamic_index_in_dim(chunks, place ^ member, axis=0, keepdims=False)
        received.append(lax.ppermute(send, axes, pairs))
    own = lax.dynamic_index_in_dim(chunks, place, axis=0, keepdims=False)
    received[0] = own
    ordered = [pick(received, place ^ member) for member in range(members)]
    while len(ordered) > 1:
        ordered = [ordered[k] + ordered[k + 1] for k in range(0, len(ordered), 2)]
    part = group_sum(ordered[0], axes, (4, 16))
    part = group_sum(part, axes, (8,))
    pieces = [part] + [
        lax.ppermute(part, axes, [(i, i ^ flip_of(member, masks)) for i in range(count)])
        for member in range(1, members)
    ]
    whole = [pick(pieces, place ^ member) for member in range(members)]
    return jnp.concatenate(whole, axis=0)


def gather_channels(block, axis):
    count = lax.axis_size(axis)
    own = [block] + [
        lax.ppermute(block, axis, [(i, (i + 2 * step) % count) for i in range(count)])
        for step in range(1, count // 2)
    ]
    own = jnp.stack(own)
    partner = lax.ppermute(own, axis, [(i, i ^ 1) for i in range(count)])
    index = lax.axis_index(axis)
    sources = jnp.stack(
        [(index - 2 * step) % count for step in range(count // 2)]
        + [((index ^ 1) - 2 * step) % count for step in range(count // 2)]
    )
    blocks = jnp.concatenate([own, partner], axis=0)
    return blocks, sources


def shift_cells(block, step_z, step_y):
    zero = jnp.zeros((), block.dtype)
    config = ((0, 0, 0), (0, 0, 0), (step_z, -step_z, 0), (0, 0, 0), (step_y, -step_y, 0))
    return lax.pad(block, zero, config)


def local(inputs, cotangent, weight):
    samples, planes, depth, channels, width = inputs.shape
    outputs = weight.shape[2]
    inputs_ext = jnp.concatenate(
        [from_behind(inputs[:, -1:], "space", 1), inputs, from_behind(inputs[:, :1], "space", -1)],
        axis=1,
    )
    blocks, sources = gather_channels(cotangent, "chan")
    count = blocks.shape[0]
    gathered = jnp.zeros(blocks.shape[1:4] + (count * channels,) + blocks.shape[5:], blocks.dtype)
    for place in range(count):
        gathered = lax.dynamic_update_slice_in_dim(gathered, blocks[place], sources[place] * channels, axis=3)
    def contribution(slab, step_x):
        first = 9 * (step_x + 1)
        total = None
        for step_y in (-1, 0, 1):
            kernel = weight[first + step_y + 1 : first + 9 : 3].reshape(3 * channels, outputs)
            product = jnp.einsum("bxzcy,kc->bxzky", slab, kernel, preferred_element_type=jnp.float32)
            for place, step_z in enumerate((-1, 0, 1)):
                part = shift_cells(product[:, :, :, place * channels : (place + 1) * channels], step_z, step_y)
                total = part if total is None else total + part
        return total

    from_prev = from_behind(contribution(gathered[:, -1:], 1), "space", 1)
    from_next = from_behind(contribution(gathered[:, :1], -1), "space", -1)
    centre = contribution(gathered, 0)
    upward = contribution(gathered[:, : planes - 1], 1)
    downward = contribution(gathered[:, 1:], -1)
    centre, upward, downward, from_prev, from_next, gathered = lax.optimization_barrier(
        (centre, upward, downward, from_prev, from_next, gathered)
    )
    stacked = jnp.concatenate(
        [shift_cells(inputs_ext, -step_z, -step_y) for step_z in (-1, 0, 1) for step_y in (-1, 0, 1)],
        axis=3,
    )
    groups = []
    for step_x in (-1, 0, 1):
        source = stacked[:, 1 + step_x : 1 + step_x + planes]
        groups.append(
            jnp.einsum("bxzky,bxzcy->kc", source, gathered, preferred_element_type=jnp.float32)
        )
    local_grad = jnp.concatenate(groups, axis=0).reshape(27, channels, outputs)
    count = samples * lax.axis_size("dp") * planes * lax.axis_size("space") * depth * width
    scale = 1.0 / math.sqrt(count)
    weight_grad = group_reduce(local_grad.reshape(-1, outputs)).reshape(local_grad.shape) * scale

    accum = (
        centre
        + jnp.concatenate([from_prev, upward], axis=1)
        + jnp.concatenate([downward, from_next], axis=1)
    )
    input_grad = accum.astype(jnp.bfloat16)
    return (input_grad, weight_grad)


def solution(mesh):
    placed = (
        P("dp", "space", None, "chan", None),
        P("dp", "space", None, "chan", None),
        P(None, "chan", None),
    )
    return jax.shard_map(
        local,
        mesh=mesh,
        in_specs=placed,
        out_specs=(P("dp", "space", None, "chan", None), P(None, "chan", None)),
        check_vma=False,
    )
```

```python
import math

import jax
import jax.numpy as jnp
from jax import lax
from jax.sharding import PartitionSpec as P


def from_behind(value, axis, steps):
    count = lax.axis_size(axis)
    initial, last = (max(0, -steps), min(count, count - steps))
    return lax.ppermute(value, axis, [(source, source + steps) for source in range(initial, last)])


def exchange_sum(value, axis, distance):
    count = lax.axis_size(axis)
    return value + lax.ppermute(value, axis, [(i, i ^ distance) for i in range(count)])


def group_sum(value, axes, masks):
    count = lax.axis_size(axes)
    index = lax.axis_index(axes)
    members = 1 << len(masks)
    place = sum(((index & mask) != 0).astype(jnp.int32) << bit for bit, mask in enumerate(masks))
    received = [value]
    for member in range(1, members):
        flip = 0
        for bit, mask in enumerate(masks):
            if member >> bit & 1:
                flip ^= mask
        received.append(lax.ppermute(value, axes, [(i, i ^ flip) for i in range(count)]))
    ordered = []
    for member in range(members):
        choice = received[0]
        for other in range(1, members):
            choice = jnp.where((place ^ member) == other, received[other], choice)
        ordered.append(choice)
    while len(ordered) > 1:
        ordered = [ordered[k] + ordered[k + 1] for k in range(0, len(ordered), 2)]
    return ordered[0]


def flip_of(member, masks):
    flip = 0
    for bit, mask in enumerate(masks):
        if member >> bit & 1:
            flip ^= mask
    return flip


def pick(choices, selector):
    choice = choices[0]
    for other in range(1, len(choices)):
        choice = jnp.where(selector == other, choices[other], choice)
    return choice


def group_reduce(value):
    axes = ("space", "dp")
    masks = (1, 2)
    count = lax.axis_size(axes)
    index = lax.axis_index(axes)
    members = 1 << len(masks)
    place = sum(((index & mask) != 0).astype(jnp.int32) << bit for bit, mask in enumerate(masks))
    chunks = value.reshape((members, -1) + value.shape[1:])
    received = [chunks[0]]
    for member in range(1, members):
        pairs = [(i, i ^ flip_of(member, masks)) for i in range(count)]
        send = lax.dynamic_index_in_dim(chunks, place ^ member, axis=0, keepdims=False)
        received.append(lax.ppermute(send, axes, pairs))
    own = lax.dynamic_index_in_dim(chunks, place, axis=0, keepdims=False)
    received[0] = own
    ordered = [pick(received, place ^ member) for member in range(members)]
    while len(ordered) > 1:
        ordered = [ordered[k] + ordered[k + 1] for k in range(0, len(ordered), 2)]
    part = group_sum(ordered[0], axes, (4, 8, 16))
    pieces = [part] + [
        lax.ppermute(part, axes, [(i, i ^ flip_of(member, masks)) for i in range(count)])
        for member in range(1, members)
    ]
    whole = [pick(pieces, place ^ member) for member in range(members)]
    return jnp.concatenate(whole, axis=0)


def gather_channels(block, axis):
    count = lax.axis_size(axis)
    own = [block] + [
        lax.ppermute(block, axis, [(i, (i + 2 * step) % count) for i in range(count)])
        for step in range(1, count // 2)
    ]
    own = jnp.stack(own)
    partner = lax.ppermute(own, axis, [(i, i ^ 1) for i in range(count)])
    index = lax.axis_index(axis)
    sources = jnp.stack(
        [(index - 2 * step) % count for step in range(count // 2)]
        + [((index ^ 1) - 2 * step) % count for step in range(count // 2)]
    )
    blocks = jnp.concatenate([own, partner], axis=0)
    return blocks, sources


def shift_cells(block, step_z, step_y):
    zero = jnp.zeros((), block.dtype)
    config = ((0, 0, 0), (0, 0, 0), (step_z, -step_z, 0), (0, 0, 0), (step_y, -step_y, 0))
    return lax.pad(block, zero, config)


def local(inputs, cotangent, weight):
    samples, planes, depth, channels, width = inputs.shape
    outputs = weight.shape[2]
    inputs_ext = jnp.concatenate(
        [from_behind(inputs[:, -1:], "space", 1), inputs, from_behind(inputs[:, :1], "space", -1)],
        axis=1,
    )
    blocks, sources = gather_channels(cotangent, "chan")
    count = blocks.shape[0]
    gathered = jnp.zeros(blocks.shape[1:4] + (count * channels,) + blocks.shape[5:], blocks.dtype)
    for place in range(count):
        gathered = lax.dynamic_update_slice_in_dim(gathered, blocks[place], sources[place] * channels, axis=3)
    contrib = {}
    for step_x in (-1, 0, 1):
        first = 9 * (step_x + 1)
        total = None
        for step_y in (-1, 0, 1):
            kernel = weight[first + step_y + 1 : first + 9 : 3].reshape(3 * channels, outputs)
            product = jnp.einsum(
                "bxzcy,kc->bxzky", gathered, kernel, preferred_element_type=jnp.float32
            )
            for place, step_z in enumerate((-1, 0, 1)):
                part = shift_cells(product[:, :, :, place * channels : (place + 1) * channels], step_z, step_y)
                total = part if total is None else total + part
        contrib[step_x] = total
    contrib, gathered = lax.optimization_barrier((contrib, gathered))
    stacked = jnp.concatenate(
        [shift_cells(inputs_ext, -step_z, -step_y) for step_z in (-1, 0, 1) for step_y in (-1, 0, 1)],
        axis=3,
    )
    groups = []
    for step_x in (-1, 0, 1):
        source = stacked[:, 1 + step_x : 1 + step_x + planes]
        groups.append(
            jnp.einsum("bxzky,bxzcy->kc", source, gathered, preferred_element_type=jnp.float32)
        )
    local_grad = jnp.concatenate(groups, axis=0).reshape(27, channels, outputs)
    count = samples * lax.axis_size("dp") * planes * lax.axis_size("space") * depth * width
    scale = 1.0 / math.sqrt(count)
    weight_grad = group_reduce(local_grad.reshape(-1, outputs)).reshape(local_grad.shape) * scale

    from_prev = from_behind(contrib[1][:, -1:], "space", 1)
    from_next = from_behind(contrib[-1][:, :1], "space", -1)
    accum = (
        contrib[0]
        + jnp.concatenate([from_prev, contrib[1][:, : planes - 1]], axis=1)
        + jnp.concatenate([contrib[-1][:, 1:], from_next], axis=1)
    )
    input_grad = accum.astype(jnp.bfloat16)
    return (input_grad, weight_grad)


def solution(mesh):
    placed = (
        P("dp", "space", None, "chan", None),
        P("dp", "space", None, "chan", None),
        P(None, "chan", None),
    )
    return jax.shard_map(
        local,
        mesh=mesh,
        in_specs=placed,
        out_specs=(P("dp", "space", None, "chan", None), P(None, "chan", None)),
        check_vma=False,
    )
```

```python
import math

import jax
import jax.numpy as jnp
from jax import lax
from jax.sharding import PartitionSpec as P


def from_behind(value, axis, steps):
    count = lax.axis_size(axis)
    initial, last = (max(0, -steps), min(count, count - steps))
    return lax.ppermute(value, axis, [(source, source + steps) for source in range(initial, last)])


def exchange_sum(value, axis, distance):
    count = lax.axis_size(axis)
    return value + lax.ppermute(value, axis, [(i, i ^ distance) for i in range(count)])


def group_sum(value, axes, masks):
    count = lax.axis_size(axes)
    index = lax.axis_index(axes)
    members = 1 << len(masks)
    place = sum(((index & mask) != 0).astype(jnp.int32) << bit for bit, mask in enumerate(masks))
    received = [value]
    for member in range(1, members):
        flip = 0
        for bit, mask in enumerate(masks):
            if member >> bit & 1:
                flip ^= mask
        received.append(lax.ppermute(value, axes, [(i, i ^ flip) for i in range(count)]))
    ordered = []
    for member in range(members):
        choice = received[0]
        for other in range(1, members):
            choice = jnp.where((place ^ member) == other, received[other], choice)
        ordered.append(choice)
    while len(ordered) > 1:
        ordered = [ordered[k] + ordered[k + 1] for k in range(0, len(ordered), 2)]
    return ordered[0]


def flip_of(member, masks):
    flip = 0
    for bit, mask in enumerate(masks):
        if member >> bit & 1:
            flip ^= mask
    return flip


def pick(choices, selector):
    choice = choices[0]
    for other in range(1, len(choices)):
        choice = jnp.where(selector == other, choices[other], choice)
    return choice


def group_reduce(value):
    axes = ("space", "dp")
    masks = (1, 2)
    count = lax.axis_size(axes)
    index = lax.axis_index(axes)
    members = 1 << len(masks)
    place = sum(((index & mask) != 0).astype(jnp.int32) << bit for bit, mask in enumerate(masks))
    chunks = value.reshape((members, -1) + value.shape[1:])
    received = [chunks[0]]
    for member in range(1, members):
        pairs = [(i, i ^ flip_of(member, masks)) for i in range(count)]
        send = lax.dynamic_index_in_dim(chunks, place ^ member, axis=0, keepdims=False)
        received.append(lax.ppermute(send, axes, pairs))
    own = lax.dynamic_index_in_dim(chunks, place, axis=0, keepdims=False)
    received[0] = own
    ordered = [pick(received, place ^ member) for member in range(members)]
    while len(ordered) > 1:
        ordered = [ordered[k] + ordered[k + 1] for k in range(0, len(ordered), 2)]
    part = group_sum(ordered[0], axes, (4, 16))
    part = group_sum(part, axes, (8,))
    pieces = [part] + [
        lax.ppermute(part, axes, [(i, i ^ flip_of(member, masks)) for i in range(count)])
        for member in range(1, members)
    ]
    whole = [pick(pieces, place ^ member) for member in range(members)]
    return jnp.concatenate(whole, axis=0)


def gather_channels(block, axis):
    count = lax.axis_size(axis)
    own = [block] + [
        lax.ppermute(block, axis, [(i, (i + 2 * step) % count) for i in range(count)])
        for step in range(1, count // 2)
    ]
    own = jnp.stack(own)
    partner = lax.ppermute(own, axis, [(i, i ^ 1) for i in range(count)])
    index = lax.axis_index(axis)
    sources = jnp.stack(
        [(index - 2 * step) % count for step in range(count // 2)]
        + [((index ^ 1) - 2 * step) % count for step in range(count // 2)]
    )
    blocks = jnp.concatenate([own, partner], axis=0)
    return blocks, sources


def shift_cells(block, step_z, step_y):
    zero = jnp.zeros((), block.dtype)
    config = ((0, 0, 0), (0, 0, 0), (step_z, -step_z, 0), (0, 0, 0), (step_y, -step_y, 0))
    return lax.pad(block, zero, config)


def local(inputs, cotangent, weight):
    samples, planes, depth, channels, width = inputs.shape
    outputs = weight.shape[2]
    inputs_ext = jnp.concatenate(
        [from_behind(inputs[:, -1:], "space", 1), inputs, from_behind(inputs[:, :1], "space", -1)],
        axis=1,
    )
    blocks, sources = gather_channels(cotangent, "chan")
    count = blocks.shape[0]
    gathered = jnp.zeros(blocks.shape[1:4] + (count * channels,) + blocks.shape[5:], blocks.dtype)
    for place in range(count):
        gathered = lax.dynamic_update_slice_in_dim(gathered, blocks[place], sources[place] * channels, axis=3)
    kernel = weight[::-1].reshape(3, 3, 3, channels, outputs)
    spread = lax.conv_general_dilated(
        gathered,
        kernel,
        window_strides=(1, 1, 1),
        padding=((2, 2), (1, 1), (1, 1)),
        dimension_numbers=("N01C2", "012OI", "N01C2"),
        preferred_element_type=jnp.float32,
    )
    spread, gathered = lax.optimization_barrier((spread, gathered))
    stacked = jnp.concatenate(
        [shift_cells(inputs_ext, -step_z, -step_y) for step_z in (-1, 0, 1) for step_y in (-1, 0, 1)],
        axis=3,
    )
    groups = []
    for step_x in (-1, 0, 1):
        source = stacked[:, 1 + step_x : 1 + step_x + planes]
        groups.append(
            jnp.einsum("bxzky,bxzcy->kc", source, gathered, preferred_element_type=jnp.float32)
        )
    local_grad = jnp.concatenate(groups, axis=0).reshape(27, channels, outputs)
    count = samples * lax.axis_size("dp") * planes * lax.axis_size("space") * depth * width
    scale = 1.0 / math.sqrt(count)
    weight_grad = group_reduce(local_grad.reshape(-1, outputs)).reshape(local_grad.shape) * scale

    from_prev = from_behind(spread[:, -1:], "space", 1)
    from_next = from_behind(spread[:, :1], "space", -1)
    inner = spread[:, 1:-1]
    accum = inner + jnp.concatenate(
        [from_prev, jnp.zeros((samples, planes - 2) + inner.shape[2:], inner.dtype), from_next], axis=1
    )
    input_grad = accum.astype(jnp.bfloat16)
    return (input_grad, weight_grad)


def solution(mesh):
    placed = (
        P("dp", "space", None, "chan", None),
        P("dp", "space", None, "chan", None),
        P(None, "chan", None),
    )
    return jax.shard_map(
        local,
        mesh=mesh,
        in_specs=placed,
        out_specs=(P("dp", "space", None, "chan", None), P(None, "chan", None)),
        check_vma=False,
    )
```

```python
import math

import jax
import jax.numpy as jnp
from jax import lax
from jax.sharding import PartitionSpec as P


def from_behind(value, axis, steps):
    count = lax.axis_size(axis)
    initial, last = (max(0, -steps), min(count, count - steps))
    return lax.ppermute(value, axis, [(source, source + steps) for source in range(initial, last)])


def exchange_sum(value, axis, distance):
    count = lax.axis_size(axis)
    return value + lax.ppermute(value, axis, [(i, i ^ distance) for i in range(count)])


def group_sum(value, axes, masks):
    count = lax.axis_size(axes)
    index = lax.axis_index(axes)
    members = 1 << len(masks)
    place = sum(((index & mask) != 0).astype(jnp.int32) << bit for bit, mask in enumerate(masks))
    received = [value]
    for member in range(1, members):
        flip = 0
        for bit, mask in enumerate(masks):
            if member >> bit & 1:
                flip ^= mask
        received.append(lax.ppermute(value, axes, [(i, i ^ flip) for i in range(count)]))
    ordered = []
    for member in range(members):
        choice = received[0]
        for other in range(1, members):
            choice = jnp.where((place ^ member) == other, received[other], choice)
        ordered.append(choice)
    while len(ordered) > 1:
        ordered = [ordered[k] + ordered[k + 1] for k in range(0, len(ordered), 2)]
    return ordered[0]


def flip_of(member, masks):
    flip = 0
    for bit, mask in enumerate(masks):
        if member >> bit & 1:
            flip ^= mask
    return flip


def pick(choices, selector):
    choice = choices[0]
    for other in range(1, len(choices)):
        choice = jnp.where(selector == other, choices[other], choice)
    return choice


def group_reduce(value):
    axes = ("space", "dp")
    masks = (1, 2)
    count = lax.axis_size(axes)
    index = lax.axis_index(axes)
    members = 1 << len(masks)
    place = sum(((index & mask) != 0).astype(jnp.int32) << bit for bit, mask in enumerate(masks))
    chunks = value.reshape((members, -1) + value.shape[1:])
    received = [chunks[0]]
    for member in range(1, members):
        pairs = [(i, i ^ flip_of(member, masks)) for i in range(count)]
        send = lax.dynamic_index_in_dim(chunks, place ^ member, axis=0, keepdims=False)
        received.append(lax.ppermute(send, axes, pairs))
    own = lax.dynamic_index_in_dim(chunks, place, axis=0, keepdims=False)
    received[0] = own
    ordered = [pick(received, place ^ member) for member in range(members)]
    while len(ordered) > 1:
        ordered = [ordered[k] + ordered[k + 1] for k in range(0, len(ordered), 2)]
    part = group_sum(ordered[0], axes, (4, 16))
    part = group_sum(part, axes, (8,))
    pieces = [part] + [
        lax.ppermute(part, axes, [(i, i ^ flip_of(member, masks)) for i in range(count)])
        for member in range(1, members)
    ]
    whole = [pick(pieces, place ^ member) for member in range(members)]
    return jnp.concatenate(whole, axis=0)


def gather_channels(block, axis):
    count = lax.axis_size(axis)
    own = [block] + [
        lax.ppermute(block, axis, [(i, (i + 2 * step) % count) for i in range(count)])
        for step in range(1, count // 2)
    ]
    own = jnp.stack(own)
    partner = lax.ppermute(own, axis, [(i, i ^ 1) for i in range(count)])
    index = lax.axis_index(axis)
    sources = jnp.stack(
        [(index - 2 * step) % count for step in range(count // 2)]
        + [((index ^ 1) - 2 * step) % count for step in range(count // 2)]
    )
    blocks = jnp.concatenate([own, partner], axis=0)
    return blocks, sources


def shift_cells(block, step_z, step_y):
    zero = jnp.zeros((), block.dtype)
    config = ((0, 0, 0), (0, 0, 0), (step_z, -step_z, 0), (0, 0, 0), (step_y, -step_y, 0))
    return lax.pad(block, zero, config)


def local(inputs, cotangent, weight):
    samples, planes, depth, channels, width = inputs.shape
    outputs = weight.shape[2]
    inputs_ext = jnp.concatenate(
        [from_behind(inputs[:, -1:], "space", 1), inputs, from_behind(inputs[:, :1], "space", -1)],
        axis=1,
    )
    blocks, sources = gather_channels(cotangent, "chan")
    count = blocks.shape[0]
    gathered = jnp.zeros(blocks.shape[1:4] + (count * channels,) + blocks.shape[5:], blocks.dtype)
    for place in range(count):
        gathered = lax.dynamic_update_slice_in_dim(gathered, blocks[place], sources[place] * channels, axis=3)
    deep = jnp.concatenate([shift_cells(gathered, step_z, 0) for step_z in (-1, 0, 1)], axis=3)
    contrib = {}
    for step_x in (-1, 0, 1):
        first = 9 * (step_x + 1)
        total = None
        for step_y in (-1, 0, 1):
            kernel = weight[first + step_y + 1 : first + 9 : 3]
            kernel = jnp.transpose(kernel, (1, 0, 2)).reshape(channels, 3 * outputs)
            product = jnp.einsum("bxzcy,kc->bxzky", deep, kernel, preferred_element_type=jnp.float32)
            part = shift_cells(product, 0, step_y)
            total = part if total is None else total + part
        contrib[step_x] = total
    contrib, gathered = lax.optimization_barrier((contrib, gathered))
    stacked = jnp.concatenate(
        [shift_cells(inputs_ext, -step_z, -step_y) for step_z in (-1, 0, 1) for step_y in (-1, 0, 1)],
        axis=3,
    )
    groups = []
    for step_x in (-1, 0, 1):
        source = stacked[:, 1 + step_x : 1 + step_x + planes]
        groups.append(
            jnp.einsum("bxzky,bxzcy->kc", source, gathered, preferred_element_type=jnp.float32)
        )
    local_grad = jnp.concatenate(groups, axis=0).reshape(27, channels, outputs)
    count = samples * lax.axis_size("dp") * planes * lax.axis_size("space") * depth * width
    scale = 1.0 / math.sqrt(count)
    weight_grad = group_reduce(local_grad.reshape(-1, outputs)).reshape(local_grad.shape) * scale

    from_prev = from_behind(contrib[1][:, -1:], "space", 1)
    from_next = from_behind(contrib[-1][:, :1], "space", -1)
    accum = (
        contrib[0]
        + jnp.concatenate([from_prev, contrib[1][:, : planes - 1]], axis=1)
        + jnp.concatenate([contrib[-1][:, 1:], from_next], axis=1)
    )
    input_grad = accum.astype(jnp.bfloat16)
    return (input_grad, weight_grad)


def solution(mesh):
    placed = (
        P("dp", "space", None, "chan", None),
        P("dp", "space", None, "chan", None),
        P(None, "chan", None),
    )
    return jax.shard_map(
        local,
        mesh=mesh,
        in_specs=placed,
        out_specs=(P("dp", "space", None, "chan", None), P(None, "chan", None)),
        check_vma=False,
    )
```

```python
import math

import jax
import jax.numpy as jnp
from jax import lax
from jax.sharding import PartitionSpec as P


def from_behind(value, axis, steps):
    count = lax.axis_size(axis)
    initial, last = (max(0, -steps), min(count, count - steps))
    return lax.ppermute(value, axis, [(source, source + steps) for source in range(initial, last)])


def group_sum(value, axes, masks):
    count = lax.axis_size(axes)
    index = lax.axis_index(axes)
    members = 1 << len(masks)
    place = sum(((index & mask) != 0).astype(jnp.int32) << bit for bit, mask in enumerate(masks))
    received = [value]
    for member in range(1, members):
        flip = 0
        for bit, mask in enumerate(masks):
            if member >> bit & 1:
                flip ^= mask
        received.append(lax.ppermute(value, axes, [(i, i ^ flip) for i in range(count)]))
    ordered = []
    for member in range(members):
        choice = received[0]
        for other in range(1, members):
            choice = jnp.where((place ^ member) == other, received[other], choice)
        ordered.append(choice)
    while len(ordered) > 1:
        ordered = [ordered[k] + ordered[k + 1] for k in range(0, len(ordered), 2)]
    return ordered[0]


def flip_of(member, masks):
    flip = 0
    for bit, mask in enumerate(masks):
        if member >> bit & 1:
            flip ^= mask
    return flip


def pick(choices, selector):
    choice = choices[0]
    for other in range(1, len(choices)):
        choice = jnp.where(selector == other, choices[other], choice)
    return choice


def group_reduce(value):
    axes = ("space", "dp")
    masks = (1, 2)
    count = lax.axis_size(axes)
    index = lax.axis_index(axes)
    members = 1 << len(masks)
    place = sum(((index & mask) != 0).astype(jnp.int32) << bit for bit, mask in enumerate(masks))
    chunks = value.reshape((members, -1) + value.shape[1:])
    received = [chunks[0]]
    for member in range(1, members):
        pairs = [(i, i ^ flip_of(member, masks)) for i in range(count)]
        send = lax.dynamic_index_in_dim(chunks, place ^ member, axis=0, keepdims=False)
        received.append(lax.ppermute(send, axes, pairs))
    own = lax.dynamic_index_in_dim(chunks, place, axis=0, keepdims=False)
    received[0] = own
    ordered = [pick(received, place ^ member) for member in range(members)]
    while len(ordered) > 1:
        ordered = [ordered[k] + ordered[k + 1] for k in range(0, len(ordered), 2)]
    part = group_sum(ordered[0], axes, (4, 16))
    part = group_sum(part, axes, (8,))
    pieces = [part] + [
        lax.ppermute(part, axes, [(i, i ^ flip_of(member, masks)) for i in range(count)])
        for member in range(1, members)
    ]
    whole = [pick(pieces, place ^ member) for member in range(members)]
    return jnp.concatenate(whole, axis=0)


def gather_channels(block, axis):
    count = lax.axis_size(axis)
    own = [block] + [
        lax.ppermute(block, axis, [(i, (i + 2 * step) % count) for i in range(count)])
        for step in range(1, count // 2)
    ]
    own = jnp.stack(own)
    partner = lax.ppermute(own, axis, [(i, i ^ 1) for i in range(count)])
    index = lax.axis_index(axis)
    sources = jnp.stack(
        [(index - 2 * step) % count for step in range(count // 2)]
        + [((index ^ 1) - 2 * step) % count for step in range(count // 2)]
    )
    blocks = jnp.concatenate([own, partner], axis=0)
    return blocks, sources


def shift_cells(block, step_z, step_y):
    zero = jnp.zeros((), block.dtype)
    config = ((0, 0, 0), (0, 0, 0), (step_z, -step_z, 0), (0, 0, 0), (step_y, -step_y, 0))
    return lax.pad(block, zero, config)


def section(inputs, cotangent, weight):
    samples, planes, depth, channels, width = inputs.shape
    outputs = weight.shape[2]
    inputs_ext = jnp.concatenate(
        [from_behind(inputs[:, -1:], "space", 1), inputs, from_behind(inputs[:, :1], "space", -1)],
        axis=1,
    )
    blocks, sources = gather_channels(cotangent, "chan")
    count = blocks.shape[0]
    gathered = jnp.zeros(blocks.shape[1:4] + (count * channels,) + blocks.shape[5:], blocks.dtype)
    for place in range(count):
        gathered = lax.dynamic_update_slice_in_dim(gathered, blocks[place], sources[place] * channels, axis=3)
    contrib = {}
    for step_x in (-1, 0, 1):
        first = 9 * (step_x + 1)
        total = None
        for step_y in (-1, 0, 1):
            kernel = weight[first + step_y + 1 : first + 9 : 3].reshape(3 * channels, outputs)
            product = jnp.einsum(
                "bxzcy,kc->bxzky", gathered, kernel, preferred_element_type=jnp.float32
            )
            for place, step_z in enumerate((-1, 0, 1)):
                part = shift_cells(product[:, :, :, place * channels : (place + 1) * channels], step_z, step_y)
                total = part if total is None else total + part
        contrib[step_x] = total
    contrib, gathered = lax.optimization_barrier((contrib, gathered))
    stacked = jnp.concatenate(
        [shift_cells(inputs_ext, -step_z, -step_y) for step_z in (-1, 0, 1) for step_y in (-1, 0, 1)],
        axis=3,
    )
    groups = []
    for step_x in (-1, 0, 1):
        source = stacked[:, 1 + step_x : 1 + step_x + planes]
        groups.append(
            jnp.einsum("bxzky,bxzcy->kc", source, gathered, preferred_element_type=jnp.float32)
        )
    local_grad = jnp.concatenate(groups, axis=0).reshape(27, channels, outputs)
    count = samples * lax.axis_size("dp") * planes * lax.axis_size("space") * depth * width
    scale = 1.0 / math.sqrt(count)
    weight_grad = group_reduce(local_grad.reshape(-1, outputs)).reshape(local_grad.shape) * scale

    from_prev = from_behind(contrib[1][:, -1:], "space", 1)
    from_next = from_behind(contrib[-1][:, :1], "space", -1)
    accum = (
        contrib[0]
        + jnp.concatenate([from_prev, contrib[1][:, : planes - 1]], axis=1)
        + jnp.concatenate([contrib[-1][:, 1:], from_next], axis=1)
    )
    input_grad = accum.astype(jnp.bfloat16)
    return (input_grad, weight_grad)


def solution(mesh):
    placed = (
        P("dp", "space", None, "chan", None),
        P("dp", "space", None, "chan", None),
        P(None, "chan", None),
    )
    return jax.shard_map(
        section,
        mesh=mesh,
        in_specs=placed,
        out_specs=(P("dp", "space", None, "chan", None), P(None, "chan", None)),
        check_vma=False,
    )
```

```python
import math

import jax
import jax.numpy as jnp
from jax import lax
from jax.sharding import PartitionSpec as P


def from_behind(value, axis, steps):
    count = lax.axis_size(axis)
    initial, last = (max(0, -steps), min(count, count - steps))
    return lax.ppermute(value, axis, [(source, source + steps) for source in range(initial, last)])


def group_sum(value, axes, masks):
    count = lax.axis_size(axes)
    index = lax.axis_index(axes)
    members = 1 << len(masks)
    place = sum(((index & mask) != 0).astype(jnp.int32) << bit for bit, mask in enumerate(masks))
    received = [value]
    for member in range(1, members):
        flip = 0
        for bit, mask in enumerate(masks):
            if member >> bit & 1:
                flip ^= mask
        received.append(lax.ppermute(value, axes, [(i, i ^ flip) for i in range(count)]))
    ordered = []
    for member in range(members):
        choice = received[0]
        for other in range(1, members):
            choice = jnp.where((place ^ member) == other, received[other], choice)
        ordered.append(choice)
    while len(ordered) > 1:
        ordered = [ordered[k] + ordered[k + 1] for k in range(0, len(ordered), 2)]
    return ordered[0]


def flip_of(member, masks):
    flip = 0
    for bit, mask in enumerate(masks):
        if member >> bit & 1:
            flip ^= mask
    return flip


def pick(choices, selector):
    choice = choices[0]
    for other in range(1, len(choices)):
        choice = jnp.where(selector == other, choices[other], choice)
    return choice


def group_reduce(value):
    axes = ("space", "dp")
    masks = (1, 2)
    count = lax.axis_size(axes)
    index = lax.axis_index(axes)
    members = 1 << len(masks)
    place = sum(((index & mask) != 0).astype(jnp.int32) << bit for bit, mask in enumerate(masks))
    chunks = value.reshape((members, -1) + value.shape[1:])
    received = [chunks[0]]
    for member in range(1, members):
        pairs = [(i, i ^ flip_of(member, masks)) for i in range(count)]
        send = lax.dynamic_index_in_dim(chunks, place ^ member, axis=0, keepdims=False)
        received.append(lax.ppermute(send, axes, pairs))
    own = lax.dynamic_index_in_dim(chunks, place, axis=0, keepdims=False)
    received[0] = own
    ordered = [pick(received, place ^ member) for member in range(members)]
    while len(ordered) > 1:
        ordered = [ordered[k] + ordered[k + 1] for k in range(0, len(ordered), 2)]
    part = group_sum(ordered[0], axes, (4, 16))
    part = group_sum(part, axes, (8,))
    pieces = [part] + [
        lax.ppermute(part, axes, [(i, i ^ flip_of(member, masks)) for i in range(count)])
        for member in range(1, members)
    ]
    whole = [pick(pieces, place ^ member) for member in range(members)]
    return jnp.concatenate(whole, axis=0)


def gather_channels(block, axis):
    count = lax.axis_size(axis)
    own = [block] + [
        lax.ppermute(block, axis, [(i, (i + 2 * step) % count) for i in range(count)])
        for step in range(1, count // 2)
    ]
    swap = [(i, i ^ 1) for i in range(count)]
    partner = jnp.concatenate(
        [lax.ppermute(block, axis, swap)[None], lax.ppermute(jnp.stack(own[1:]), axis, swap)], axis=0
    )
    own = jnp.stack(own)
    index = lax.axis_index(axis)
    sources = jnp.stack(
        [(index - 2 * step) % count for step in range(count // 2)]
        + [((index ^ 1) - 2 * step) % count for step in range(count // 2)]
    )
    blocks = jnp.concatenate([own, partner], axis=0)
    return blocks, sources


def shift_cells(block, step_z, step_y):
    zero = jnp.zeros((), block.dtype)
    config = ((0, 0, 0), (0, 0, 0), (step_z, -step_z, 0), (0, 0, 0), (step_y, -step_y, 0))
    return lax.pad(block, zero, config)


def section(inputs, cotangent, weight):
    samples, planes, depth, channels, width = inputs.shape
    outputs = weight.shape[2]
    inputs_ext = jnp.concatenate(
        [from_behind(inputs[:, -1:], "space", 1), inputs, from_behind(inputs[:, :1], "space", -1)],
        axis=1,
    )
    blocks, sources = gather_channels(cotangent, "chan")
    count = blocks.shape[0]
    gathered = jnp.zeros(blocks.shape[1:4] + (count * channels,) + blocks.shape[5:], blocks.dtype)
    for place in range(count):
        gathered = lax.dynamic_update_slice_in_dim(gathered, blocks[place], sources[place] * channels, axis=3)
    contrib = {}
    for step_x in (-1, 0, 1):
        first = 9 * (step_x + 1)
        total = None
        for step_y in (-1, 0, 1):
            kernel = weight[first + step_y + 1 : first + 9 : 3].reshape(3 * channels, outputs)
            product = jnp.einsum(
                "bxzcy,kc->bxzky", gathered, kernel, preferred_element_type=jnp.float32
            )
            for place, step_z in enumerate((-1, 0, 1)):
                part = shift_cells(product[:, :, :, place * channels : (place + 1) * channels], step_z, step_y)
                total = part if total is None else total + part
        contrib[step_x] = total
    contrib, gathered = lax.optimization_barrier((contrib, gathered))
    stacked = jnp.concatenate(
        [shift_cells(inputs_ext, -step_z, -step_y) for step_z in (-1, 0, 1) for step_y in (-1, 0, 1)],
        axis=3,
    )
    groups = []
    for step_x in (-1, 0, 1):
        source = stacked[:, 1 + step_x : 1 + step_x + planes]
        groups.append(
            jnp.einsum("bxzky,bxzcy->kc", source, gathered, preferred_element_type=jnp.float32)
        )
    local_grad = jnp.concatenate(groups, axis=0).reshape(27, channels, outputs)
    count = samples * lax.axis_size("dp") * planes * lax.axis_size("space") * depth * width
    scale = 1.0 / math.sqrt(count)
    weight_grad = group_reduce(local_grad.reshape(-1, outputs)).reshape(local_grad.shape) * scale

    from_prev = from_behind(contrib[1][:, -1:], "space", 1)
    from_next = from_behind(contrib[-1][:, :1], "space", -1)
    accum = (
        contrib[0]
        + jnp.concatenate([from_prev, contrib[1][:, : planes - 1]], axis=1)
        + jnp.concatenate([contrib[-1][:, 1:], from_next], axis=1)
    )
    input_grad = accum.astype(jnp.bfloat16)
    return (input_grad, weight_grad)


def solution(mesh):
    placed = (
        P("dp", "space", None, "chan", None),
        P("dp", "space", None, "chan", None),
        P(None, "chan", None),
    )
    return jax.shard_map(
        section,
        mesh=mesh,
        in_specs=placed,
        out_specs=(P("dp", "space", None, "chan", None), P(None, "chan", None)),
        check_vma=False,
    )
```
